32 devices in a mesh: groups: 2 (over y), tm: 16 (over z, x, core).
Axes of the slice: x: 2, y: 2, z: 4, core: 2. Of those that a mesh axis runs over, the one named last changes fastest.
Arguments:
- noisy: bfloat16 [256, 16, 16, 256], P(('groups', 'tm')), parts along dimension 0, may hold values from -6 to 6
- observed: float32 [256, 16, 256], P(('groups', 'tm')), parts along dimension 0, may hold values from -6 to 6
- obs_mask: int32 [256, 16, 256], P(('groups', 'tm')), parts along dimension 0, may hold values 0 or 1
- obs_channel: int32 [256, 16, 256], P(('groups', 'tm')), parts along dimension 0, may hold values from 0 to 15
- step_index: int32 [2], P('groups'), parts along dimension 0, may hold values from 0 to 63
- w_first: bfloat16 [128, 80, 3, 3], replicated, may hold values from -0.21875 to 0.21875
- b_first: float32 [128], replicated, may hold values from -3 to 3
- w_second: bfloat16 [16, 128, 3, 3], replicated, may hold values from -0.1875 to 0.1875
- b_second: float32 [16], replicated, may hold values from -3 to 3
Outputs:
- guided: float32 [256, 16, 16, 256], P(('groups', 'tm')), parts along dimension 0
The draws below stay inside these ranges and needn't reach their ends.
There are 2 independent parts, one for each index of `groups`. The reference program is written for one: setup_inputs(seed, part) draws one part's arguments, and reference() takes and returns one part's arrays. A program takes and returns all parts, laid end to end along the dimension named above; an argument that names none is the same for every part. Nothing has to cross between parts.
All inputs are finite; a program needn't handle non-finite values. No bound on the sum of `obs_mask` on one device may be relied on, other than what follows from the above.
Results may differ from the reference program's by a relative error of at most 0.0015.
Values may be sent and summed in bfloat16 or wider, within the bound.
No kernel may reach another device: no remote copies, remote signals or barrier semaphores. Data moves between devices by JAX's collectives and lax.ppermute only.
A program may use at most 128 MiB of HBM per device.

```python
import jax
import jax.numpy as jnp
from jax import lax

C = 16
HID = 128
WIN = 5
STEPS = 64
ROWS = 16
COLS = 256
FRAMES = 128


def place_ends(entries, key, least, largest):
    extent = entries.shape
    spot = [jax.random.randint(jax.random.fold_in(key, axis), (), 0, extent[axis]) for axis in range(len(extent))]
    entries = entries.at[tuple(spot)].set(least)
    longest = extent.index(max(extent))
    spot[longest] = (spot[longest] + 1) % extent[longest]
    return entries.at[tuple(spot)].set(largest)


def levels(own_key, dims, shards, least, largest):
    def one(axis_at, blocks):
        draws = jax.random.uniform(jax.random.fold_in(jax.random.fold_in(own_key, 6), axis_at), (blocks,), jnp.float32, least / len(shards), largest / len(shards))
        return jnp.repeat(jnp.exp(draws), dims[axis_at] // blocks).reshape((-1,) + (1,) * (len(dims) - axis_at - 1))

    gain = one(*shards[0])
    for cut in shards[1:]:
        gain = gain * one(*cut)
    return gain


def normal_values(rng, extent, deviation, reach, shards=(), held_as=jnp.bfloat16):
    gain = levels(rng, extent, shards, -0.22, 0.18) if shards else 1.0
    drawn = jax.random.normal(rng, extent, jnp.float32) * deviation * gain
    return jnp.minimum(jnp.maximum(drawn, -reach), reach).astype(held_as)


def setup_inputs(seed: int = 0, part: int = 0) -> dict:
    arg_keys = jax.random.split(jax.random.key(seed), 10)
    part_splits = jax.random.split(jax.random.fold_in(arg_keys[9], part), 10)
    return {
        "noisy": normal_values(part_splits[0], (FRAMES, C, ROWS, COLS), 1.0, 6.0, ((0, 16),)),
        "observed": normal_values(part_splits[1], (FRAMES, ROWS, COLS), 1.0, 6.0, ((0, 16),), jnp.float32),
        "obs_mask": place_ends((jax.random.randint(part_splits[2], (FRAMES, ROWS, COLS), 0, 2) < 1).astype(jnp.int32), jax.random.fold_in(part_splits[2], 1), 0, 1),
        "obs_channel": place_ends(jax.random.randint(part_splits[3], (FRAMES, ROWS, COLS), 0, C), jax.random.fold_in(part_splits[3], 1), 0, C - 1).astype(jnp.int32),
        "step_index": jax.random.randint(part_splits[4], (1,), 0, STEPS).astype(jnp.int32),
        "w_first": normal_values(arg_keys[5], (HID, WIN * C, 3, 3), (9 * WIN * C) ** -0.5, 0.21875),
        "b_first": normal_values(arg_keys[6], (HID,), 0.5, 3.0, (), jnp.float32),
        "w_second": normal_values(arg_keys[7], (C, HID, 3, 3), (9 * HID) ** -0.5, 0.1875),
        "b_second": normal_values(arg_keys[8], (C,), 0.5, 3.0, (), jnp.float32),
    }


sigma_low = 0.1
sigma_ratio = 20.0

def conv(value, kernel):
    return lax.conv_general_dilated(value.astype(jnp.float32), kernel.astype(jnp.float32), (1, 1), ((1, 1), (1, 1)), dimension_numbers=('NCHW', 'OIHW', 'NCHW'), precision=lax.Precision.HIGHEST)

def conv_back(grad, kernel):
    flipped = jnp.transpose(kernel, (1, 0, 2, 3))[:, :, ::-1, ::-1]
    return conv(grad, flipped)

def reference(noisy, observed, obs_mask, obs_channel, step_index, w_first, b_first, w_second, b_second):
    frames = noisy.shape[0]
    chans = noisy.shape[1]
    level = step_index[0].astype(jnp.float32) / jnp.float32(STEPS - 1)
    sigma = jnp.float32(sigma_low) * jnp.exp(jnp.log(jnp.float32(sigma_ratio)) * level)
    c_in = 1.0 / jnp.sqrt(1.0 + sigma * sigma)
    weight_obs = 1.0 / (1.0 + sigma * sigma)
    scaled = (c_in * noisy.astype(jnp.float32)).astype(jnp.bfloat16)
    padded = jnp.pad(scaled, ((2, 2), (0, 0), (0, 0), (0, 0)))
    channel_ids = jnp.arange(chans, dtype=jnp.int32)
    select = ((obs_channel[:, None, :, :] == channel_ids[None, :, None, None]) & (obs_mask[:, None, :, :] == 1)).astype(jnp.float32)
    zero = jnp.int32(0)

    def frame_step(index, carry):
        back_pad, den_all, misfit_all = carry
        tpos = jnp.asarray(index).astype(jnp.int32)
        window = lax.dynamic_slice(padded, (tpos, zero, zero, zero), (WIN, chans, ROWS, COLS)).reshape(1, WIN * chans, ROWS, COLS)
        pre = conv(window, w_first)[0] + b_first[:, None, None]
        hidden = jax.nn.silu(pre).astype(jnp.bfloat16)
        den = noisy[tpos].astype(jnp.float32) + conv(hidden[None], w_second)[0] + b_second[:, None, None]
        misfit = select[tpos] * (den - observed[tpos][None])
        misfit_b = misfit.astype(jnp.bfloat16)
        sig = jax.nn.sigmoid(pre)
        grad_hidden = (conv_back(misfit_b[None], w_second)[0] * (sig * (1.0 + pre * (1.0 - sig)))).astype(jnp.bfloat16)
        grad_window = conv_back(grad_hidden[None], w_first)[0].reshape(WIN, chans, ROWS, COLS)
        old = lax.dynamic_slice(back_pad, (tpos, zero, zero, zero), (WIN, chans, ROWS, COLS))
        back_pad = lax.dynamic_update_slice(back_pad, old + grad_window, (tpos, zero, zero, zero))
        den_all = lax.dynamic_update_slice(den_all, den[None], (tpos, zero, zero, zero))
        misfit_all = lax.dynamic_update_slice(misfit_all, misfit[None], (tpos, zero, zero, zero))
        return (back_pad, den_all, misfit_all)
    start = (jnp.zeros((frames + 4, chans, ROWS, COLS), jnp.float32), jnp.zeros((frames, chans, ROWS, COLS), jnp.float32), jnp.zeros((frames, chans, ROWS, COLS), jnp.float32))
    back_pad, den_all, misfit_all = lax.fori_loop(0, frames, frame_step, start)
    back = back_pad[2:frames + 2]
    return den_all - weight_obs * (misfit_all + c_in * back)
```

```python
import functools

import jax
import jax.numpy as jnp
from jax import lax
from jax.experimental import pallas as pl
from jax.experimental.pallas import tpu as pltpu
from jax.sharding import PartitionSpec as P

STEPS = 64
ROWS = 16
COLS = 256


sigma_low = 0.1
sigma_ratio = 20.0


def with_halo(x, sides, width):
    for axis, dim in sides:
        peers, length = (lax.axis_size(axis), x.shape[dim])
        up = [(i, (i + 1) % peers) for i in range(peers - 1)]
        down = [(j, i) for i, j in up]
        last = lax.slice_in_dim(x, length - width, length, axis=dim)
        initial = lax.slice_in_dim(x, 0, width, axis=dim)
        before = lax.ppermute(last, axis, up)
        after = lax.ppermute(initial, axis, down)
        x = jnp.concatenate([before, x, after], axis=dim)
    return x


def passed_along(value, axis, steps):
    count = lax.axis_size(axis)
    initial, last = (max(0, -steps), min(count, count - steps))
    return lax.ppermute(value, axis, [(source, source + steps) for source in range(initial, last)])


def frame_kernel(
    sc_ref, ext_ref, noisy_ref, obs_ref, mask_ref, chan_ref,
    w1_ref, b1_ref, w2z_ref, b2_ref, w2t_ref, w1t_ref,
    a_ref, back_ref,
):
    f32, bf16 = jnp.float32, jnp.bfloat16
    t = pl.program_id(0)
    chans = noisy_ref.shape[1]
    pix = noisy_ref.shape[2]
    span = w1_ref.shape[2] // (3 * chans)

    @pl.when(t == 0)
    def _():
        back_ref[...] = jnp.zeros_like(back_ref)

    lane = lax.broadcasted_iota(jnp.int32, (1, pix), 1)
    col = lane % COLS

    def shift_x(v, d):
        if d == 0:
            return v
        r = pltpu.roll(v, (-d) % pix, 1)
        ok = (col + d >= 0) & (col + d < COLS)
        return jnp.where(ok, r, jnp.zeros_like(r))

    def shift_y(v, d):
        if d == 0:
            return v
        z = jnp.zeros((v.shape[0], COLS * abs(d)), v.dtype)
        if d > 0:
            return jnp.concatenate([v[:, d * COLS :], z], axis=1)
        return jnp.concatenate([z, v[:, : d * COLS]], axis=1)

    win = jnp.concatenate([ext_ref[t + k] for k in range(span)], axis=0).astype(f32)
    xcat = jnp.concatenate([shift_x(win, b - 1).astype(bf16) for b in range(3)], axis=0)
    pre = None
    for a in range(3):
        d = jnp.dot(w1_ref[a], shift_y(xcat, a - 1), preferred_element_type=f32)
        pre = d if pre is None else pre + d
    pre = pre + b1_ref[...]
    sig = 1.0 / (1.0 + jnp.exp(-pre))
    hidden = (pre * sig).astype(bf16)
    deriv = sig * (1.0 + pre * (1.0 - sig))

    z = jnp.dot(w2z_ref[...], hidden, preferred_element_type=f32)
    conv2 = None
    for b in range(3):
        s = None
        for a in range(3):
            r0 = (a * 3 + b) * chans
            v = shift_y(z[r0 : r0 + chans], a - 1)
            s = v if s is None else s + v
        s = shift_x(s, b - 1)
        conv2 = s if conv2 is None else conv2 + s
    den = noisy_ref[0].astype(f32) + conv2 + b2_ref[...]

    cid = lax.broadcasted_iota(jnp.int32, (chans, pix), 0)
    sel = (chan_ref[0] == cid) & (mask_ref[0] == 1)
    misfit = jnp.where(sel, den - obs_ref[0], 0.0)
    a_ref[0] = den - sc_ref[1] * misfit

    mb = misfit.astype(bf16).astype(f32)
    g = jnp.concatenate(
        [shift_x(shift_y(mb, 1 - a), 1 - b).astype(bf16) for a in range(3) for b in range(3)],
        axis=0,
    )
    ghp = jnp.dot(w2t_ref[...], g, preferred_element_type=f32)
    gh = (ghp * deriv).astype(bf16).astype(f32)

    hcat = jnp.concatenate([shift_x(gh, 1 - b).astype(bf16) for b in range(3)], axis=0)
    gw = None
    for a in range(3):
        d = jnp.dot(w1t_ref[a], shift_y(hcat, 1 - a), preferred_element_type=f32)
        gw = d if gw is None else gw + d
    for k in range(span):
        back_ref[t + k] += gw[k * chans : (k + 1) * chans]


def per_device(
    noisy, observed, obs_mask, obs_channel, step_index, w_first, b_first, w_second, b_second
):
    frames = noisy.shape[0]
    chans = noisy.shape[1]
    hid = w_first.shape[0]
    span = w_first.shape[1] // chans
    half = span // 2
    pix = ROWS * COLS
    level = step_index[0].astype(jnp.float32) / jnp.float32(STEPS - 1)
    sigma = jnp.float32(sigma_low) * jnp.exp(jnp.log(jnp.float32(sigma_ratio)) * level)
    c_in = 1.0 / jnp.sqrt(1.0 + sigma * sigma)
    weight_obs = 1.0 / (1.0 + sigma * sigma)
    scaled = (c_in * noisy.astype(jnp.float32)).astype(jnp.bfloat16)
    extended = with_halo(scaled, (("tm", 0),), half).reshape(frames + 2 * half, chans, pix)

    w1 = jnp.transpose(w_first, (2, 0, 3, 1)).reshape(3, hid, 3 * span * chans)
    w1t = jnp.transpose(w_first, (2, 1, 3, 0)).reshape(3, span * chans, 3 * hid)
    w2z = jnp.transpose(w_second, (2, 3, 0, 1)).reshape(9 * chans, hid)
    w2t = jnp.transpose(w_second, (1, 2, 3, 0)).reshape(hid, 9 * chans)
    sc = jnp.stack([c_in, weight_obs]).astype(jnp.float32)

    full = lambda shape: pl.BlockSpec(shape, lambda t: (0,) * len(shape))
    frame = lambda shape: pl.BlockSpec(shape, lambda t: (t,) + (0,) * (len(shape) - 1))
    a_part, back_pad = pl.pallas_call(
        frame_kernel,
        grid=(frames,),
        in_specs=[
            pl.BlockSpec(memory_space=pltpu.SMEM),
            full((frames + 2 * half, chans, pix)),
            frame((1, chans, pix)),
            frame((1, 1, pix)),
            frame((1, 1, pix)),
            frame((1, 1, pix)),
            full(w1.shape),
            full((hid, 1)),
            full(w2z.shape),
            full((chans, 1)),
            full(w2t.shape),
            full(w1t.shape),
        ],
        out_specs=[
            frame((1, chans, pix)),
            full((frames + 2 * half, chans, pix)),
        ],
        out_shape=[
            jax.ShapeDtypeStruct((frames, chans, pix), jnp.float32),
            jax.ShapeDtypeStruct((frames + 2 * half, chans, pix), jnp.float32),
        ],
        compiler_params=pltpu.CompilerParams(dimension_semantics=("arbitrary",)),
    )(
        sc,
        extended,
        noisy.reshape(frames, chans, pix),
        observed.reshape(frames, 1, pix),
        obs_mask.reshape(frames, 1, pix),
        obs_channel.reshape(frames, 1, pix),
        w1,
        b_first.reshape(hid, 1),
        w2z,
        b_second.reshape(chans, 1),
        w2t,
        w1t,
    )
    from_right = passed_along(back_pad[:half].astype(jnp.bfloat16), "tm", -1).astype(jnp.float32)
    from_left = passed_along(back_pad[frames + half :].astype(jnp.bfloat16), "tm", 1).astype(
        jnp.float32
    )
    back = back_pad[half : frames + half]
    back = back.at[frames - half :].add(from_right)
    back = back.at[:half].add(from_left)
    guided = a_part - (weight_obs * c_in) * back
    return guided.reshape(noisy.shape)


def solution(mesh):
    return jax.shard_map(
        per_device,
        mesh=mesh,
        in_specs=(
            P(("groups", "tm"), None, None, None),
            P(("groups", "tm"), None, None),
            P(("groups", "tm"), None, None),
            P(("groups", "tm"), None, None),
            P("groups"),
            P(),
            P(),
            P(),
            P(),
        ),
        out_specs=P(("groups", "tm"), None, None, None),
        check_vma=False,
    )
```
